32 devices in a mesh: outer: 4 (over z), inner: 2 (over x), tensor: 4 (over y, core).
Axes of the slice: x: 2, y: 2, z: 4, core: 2. Of those that a mesh axis runs over, the one named last changes fastest.
Arguments:
- hidden_in: bfloat16 [16, 577, 1024], P(('outer', 'inner')), may hold values from -6 to 6
- ln1_gain: float32 [1024], replicated, may hold values from 0.5 to 1.5
- ln1_shift: float32 [1024], replicated, may hold values from -1.5 to 1.5
- w_qkv: bfloat16 [1024, 3, 1024], P(None, None, 'tensor'), may hold values from -0.1875 to 0.1875
- qkv_bias: float32 [2, 1024], P(None, 'tensor'), may hold values from -1.5 to 1.5
- w_out: bfloat16 [1024, 1024], P('tensor'), may hold values from -0.75 to 0.75
- out_bias: float32 [1024], replicated, may hold values from -1.5 to 1.5
- ln2_gain: float32 [1024], replicated, may hold values from 0.5 to 1.5
- ln2_shift: float32 [1024], replicated, may hold values from -1.5 to 1.5
- w_fc1: bfloat16 [1024, 4096], P(None, 'tensor'), may hold values from -0.1875 to 0.1875
- fc1_bias: float32 [4096], P('tensor'), may hold values from -1.5 to 1.5
- w_fc2: bfloat16 [4096, 1024], P('tensor'), may hold values from -0.09375 to 0.09375
- fc2_bias: float32 [1024], replicated, may hold values from -1.5 to 1.5
- flags: int32 [16], P(('outer', 'inner')), may hold values 0 or 1
- out_grad: bfloat16 [16, 577, 1024], P(('outer', 'inner')), may hold values from -6 to 6
Outputs:
- block_out: bfloat16 [16, 577, 1024], P(('outer', 'inner'))
- in_grad: bfloat16 [16, 577, 1024], P(('outer', 'inner'))
- g_ln1_gain: float32 [1024], replicated
- g_ln1_shift: float32 [1024], replicated
- g_w_qkv: float32 [1024, 3, 1024], P(None, None, 'tensor')
- g_qkv_bias: float32 [2, 1024], P(None, 'tensor')
- g_w_out: float32 [1024, 1024], P('tensor')
- g_out_bias: float32 [1024], replicated
- g_ln2_gain: float32 [1024], replicated
- g_ln2_shift: float32 [1024], replicated
- g_w_fc1: float32 [1024, 4096], P(None, 'tensor')
- g_fc1_bias: float32 [4096], P('tensor')
- g_w_fc2: float32 [4096, 1024], P('tensor')
- g_fc2_bias: float32 [1024], replicated
The draws below stay inside these ranges and needn't reach their ends.
Inputs may be any that keep to these rules, and one draw needn't show every extreme that they name: `flags`: 1 marks an image, 0 a padded slot.
All inputs are finite; a program needn't handle non-finite values. No bound on the sum of `flags` on one device may be relied on, other than what follows from the above.
Results may differ from the reference program's by a relative error of at most 0.012.
Values sent between devices are 32-bit elements; how exact they have to be, the bound alone decides.
No kernel may reach another device: no remote copies, remote signals or barrier semaphores. Data moves between devices by JAX's collectives and lax.ppermute only.
A program may use at most 192 MiB of HBM per device.

```python
import jax
import jax.numpy as jnp
from jax import lax

D = 1024
HEADS = 16
HD = 64
FF = 4096
SEQ = 577
IMAGES = 16


def with_ends(array, stream_key, low, top_value):
    extent = array.shape
    place = [jax.random.randint(jax.random.fold_in(stream_key, axis), (), 0, extent[axis]) for axis in range(len(extent))]
    array = array.at[tuple(place)].set(low)
    longest = extent.index(max(extent))
    place[longest] = (place[longest] + 1) % extent[longest]
    return array.at[tuple(place)].set(top_value)


def block_scale(stream_key, shape, cuts, low, high):
    def one(position, parts):
        draws = jax.random.uniform(jax.random.fold_in(jax.random.fold_in(stream_key, 6), position), (parts,), jnp.float32, low / len(cuts), high / len(cuts))
        return jnp.repeat(jnp.exp(draws), shape[position] // parts).reshape((-1,) + (1,) * (len(shape) - position - 1))

    level = one(*cuts[0])
    for cut in cuts[1:]:
        level = level * one(*cut)
    return level


def noise(own_key, dims, spread, most, cuts=(), kind=jnp.bfloat16):
    result = jax.random.normal(own_key, dims, jnp.float32) * spread
    if len(cuts) > 0:
        result = block_scale(own_key, dims, cuts, -0.22, 0.18) * result
    return jnp.clip(result, min=-most, max=most).astype(kind)


def setup_inputs(seed: int = 0) -> dict:
    key_list = jax.random.split(jax.random.key(seed), 16)
    hidden_in = noise(key_list[0], (IMAGES, SEQ, D), 1.0, 6.0, ((0, 8),))
    ln1_gain = jnp.clip(1.0 + 0.1 * jax.random.normal(key_list[1], (D,), jnp.float32), 0.5, 1.5)
    ln1_shift = noise(key_list[2], (D,), 0.3, 1.5, (), jnp.float32)
    w_qkv = noise(key_list[3], (D, 3, D), D ** -0.5, 0.1875, ((2, 4),))
    qkv_bias = noise(key_list[4], (2, D), 0.3, 1.5, ((1, 4),), jnp.float32)
    w_out = noise(key_list[5], (D, D), (D // 16) ** -0.5, 0.75, ((0, 4),))
    out_bias = noise(key_list[6], (D,), 0.3, 1.5, (), jnp.float32)
    ln2_gain = jnp.clip(1.0 + 0.1 * jax.random.normal(key_list[7], (D,), jnp.float32), 0.5, 1.5)
    ln2_shift = noise(key_list[8], (D,), 0.3, 1.5, (), jnp.float32)
    w_fc1 = noise(key_list[9], (D, FF), D ** -0.5, 0.1875, ((1, 4),))
    fc1_bias = noise(key_list[10], (FF,), 0.3, 1.5, ((0, 4),), jnp.float32)
    w_fc2 = noise(key_list[11], (FF, D), FF ** -0.5, 0.09375, ((0, 4),))
    fc2_bias = noise(key_list[12], (D,), 0.3, 1.5, (), jnp.float32)
    flags = with_ends((jax.random.randint(key_list[13], (IMAGES,), 0, 8) < 7).astype(jnp.int32), jax.random.fold_in(key_list[13], 1), 0, 1)
    out_grad = noise(key_list[14], (IMAGES, SEQ, D), 1.0, 6.0, ((0, 8),))
    return {"hidden_in": hidden_in, "ln1_gain": ln1_gain, "ln1_shift": ln1_shift, "w_qkv": w_qkv, "qkv_bias": qkv_bias, "w_out": w_out, "out_bias": out_bias, "ln2_gain": ln2_gain, "ln2_shift": ln2_shift, "w_fc1": w_fc1, "fc1_bias": fc1_bias, "w_fc2": w_fc2, "fc2_bias": fc2_bias, "flags": flags, "out_grad": out_grad}


@jax.custom_vjp
def low(v):
    return lax.optimization_barrier(v.astype(jnp.bfloat16)).astype(jnp.float32)

@jax.custom_vjp
def low_back(v):
    return v

def low_keep(v):
    return (low(v), None)

def low_pass(kept, grad):
    return (grad,)

def back_keep(v):
    return (v, None)

def back_low(kept, grad):
    return (low(grad),)
low.defvjp(low_keep, low_pass)
low_back.defvjp(back_keep, back_low)
norm_eps = 1e-05
highest = lax.Precision.HIGHEST

def matmul(left, right):
    return jnp.dot(left, right, precision=highest)

def layer_norm(values_in, gain_vec, shift_vec):
    row_mean = lax.optimization_barrier(jnp.mean(values_in, axis=-1, keepdims=True))
    centered = values_in - row_mean
    row_var = lax.optimization_barrier(jnp.mean(centered * centered, axis=-1, keepdims=True))
    return centered * lax.rsqrt(row_var + norm_eps) * gain_vec + shift_vec

def quick_gelu(values_in):
    return values_in * jax.nn.sigmoid(1.702 * values_in)

def forward(one_image, params):
    ln1_gain, ln1_shift, w_qkv, qkv_bias, w_out, out_bias, ln2_gain, ln2_shift, w_fc1, fc1_bias, w_fc2, fc2_bias = params
    normed1 = low(layer_norm(one_image, ln1_gain, ln1_shift))
    projected = matmul(normed1, w_qkv.reshape(D, 3 * D)).reshape(SEQ, 3, D)
    q_heads = low(low_back(projected[:, 0] + qkv_bias[0])).reshape(SEQ, HEADS, HD)
    k_heads = low(low_back(projected[:, 1])).reshape(SEQ, HEADS, HD)
    v_heads = low(low_back(projected[:, 2] + qkv_bias[1])).reshape(SEQ, HEADS, HD)
    scores = jnp.einsum('qhd,khd->hqk', q_heads, k_heads, precision=highest) * HD ** (-0.5)
    scores = low_back(scores)
    attn_probs = low(jax.nn.softmax(scores, axis=-1))
    attended = jnp.einsum('hqk,khd->qhd', attn_probs, v_heads, precision=highest).reshape(SEQ, D)
    attended = low(low_back(attended))
    resid_mid = one_image + low_back(matmul(attended, w_out)) + out_bias
    normed2 = low(layer_norm(resid_mid, ln2_gain, ln2_shift))
    pre_act = low_back(matmul(normed2, w_fc1) + fc1_bias)
    gelu_out = low(quick_gelu(pre_act))
    return resid_mid + low_back(matmul(gelu_out, w_fc2)) + fc2_bias

def reference(hidden_in, ln1_gain, ln1_shift, w_qkv, qkv_bias, w_out, out_bias, ln2_gain, ln2_shift, w_fc1, fc1_bias, w_fc2, fc2_bias, flags, out_grad):
    params = (ln1_gain, ln1_shift, w_qkv.astype(jnp.float32), qkv_bias, w_out.astype(jnp.float32), out_bias, ln2_gain, ln2_shift, w_fc1.astype(jnp.float32), fc1_bias, w_fc2.astype(jnp.float32), fc2_bias)
    zero_grads = jax.tree.map(jnp.zeros_like, params)

    def step(grad_total, slot_item):
        one_image, cotangent, slot_flag = slot_item
        block_value, pullback = jax.vjp(forward, one_image.astype(jnp.float32), params)
        grad_image, grad_params = pullback(cotangent.astype(jnp.float32) * slot_flag.astype(jnp.float32))
        grad_total = jax.tree.map(lambda first, second: first + second, grad_total, grad_params)
        return (grad_total, (block_value.astype(jnp.bfloat16), grad_image.astype(jnp.bfloat16)))
    grad_total, outputs = lax.scan(step, zero_grads, (hidden_in, out_grad, flags))
    block_out, in_grad = outputs
    return (block_out, in_grad, grad_total[0], grad_total[1], grad_total[2], grad_total[3], grad_total[4], grad_total[5], grad_total[6], grad_total[7], grad_total[8], grad_total[9], grad_total[10], grad_total[11])
```

```python
import functools

import jax
import jax.numpy as jnp
from jax import lax
from jax.sharding import PartitionSpec as P

HD = 64


norm_eps = 1e-05


def layer_norm(values_in, gain_vec, shift_vec):
    row_mean = jnp.mean(values_in, axis=-1, keepdims=True)
    centered = values_in - row_mean
    row_var = jnp.mean(centered * centered, axis=-1, keepdims=True)
    return centered * lax.rsqrt(row_var + norm_eps) * gain_vec + shift_vec


def quick_gelu(values_in):
    return values_in * jax.nn.sigmoid(1.702 * values_in)


def gelu_slope(values_in):
    sig_val = jax.nn.sigmoid(1.702 * values_in)
    return sig_val + 1.702 * values_in * sig_val * (1.0 - sig_val)


def mat_prod(left, right):
    return jnp.dot(left, right, preferred_element_type=jnp.float32)


def left_contract(left, right):
    return lax.dot_general(
        left, right, (((0,), (0,)), ((), ())), preferred_element_type=jnp.float32
    )


def right_contract(left, right):
    return lax.dot_general(
        left, right, (((1,), (1,)), ((), ())), preferred_element_type=jnp.float32
    )


def col_sum(values_in):
    return jnp.sum(values_in.astype(jnp.float32), axis=0)


def attn_scores(q_heads, k_heads, score_scale):
    return (
        jnp.einsum("bqhd,bkhd->bhqk", q_heads, k_heads, preferred_element_type=jnp.float32)
        * score_scale
    )


def tensor_sum(make, width, n_tensor):
    if n_tensor == 1:
        return make(0, width)
    if n_tensor == 2:
        part = make(0, width)
        return part + lax.ppermute(part, "tensor", [(i, i ^ 1) for i in range(2)])
    if n_tensor != 4 or width % 256:
        return lax.psum(make(0, width), "tensor")
    low_bit = lax.axis_index("tensor") % 2
    half = width // 2
    keep = make(low_bit * half, half)
    send = make((1 - low_bit) * half, half)
    near = [(i, i ^ 1) for i in range(4)]
    far = [(i, i ^ 2) for i in range(4)]
    part = keep + lax.ppermute(send, "tensor", near)
    total = part + lax.ppermute(part, "tensor", far)
    back = lax.ppermute(total, "tensor", near)
    first = jnp.where(low_bit == 0, total, back)
    second = jnp.where(low_bit == 0, back, total)
    return jnp.concatenate([first, second], axis=1)


def cols(weight, start, size, axis):
    return lax.dynamic_slice_in_dim(weight, start, size, axis)


def per_device(
    n_tensor,
    hidden_in,
    ln1_gain,
    ln1_shift,
    w_qkv,
    qkv_bias,
    w_out,
    out_bias,
    ln2_gain,
    ln2_shift,
    w_fc1,
    fc1_bias,
    w_fc2,
    fc2_bias,
    flags,
    out_grad,
):
    img_count, seq_len, model_width = hidden_in.shape
    row_count = img_count * seq_len
    head_cols = w_qkv.shape[2]
    head_count = head_cols // HD
    score_scale = HD ** (-0.5)
    head_shape = (img_count, seq_len, head_count, HD)
    qkv_flat = w_qkv.reshape(model_width, 3 * head_cols)
    x_rows = hidden_in.reshape(row_count, model_width).astype(jnp.float32)
    normed1 = layer_norm(x_rows, ln1_gain, ln1_shift).astype(jnp.bfloat16)
    projected = mat_prod(normed1, qkv_flat).reshape(row_count, 3, head_cols)
    q_heads = (projected[:, 0] + qkv_bias[0]).astype(jnp.bfloat16).reshape(head_shape)
    k_heads = projected[:, 1].astype(jnp.bfloat16).reshape(head_shape)
    v_heads = (projected[:, 2] + qkv_bias[1]).astype(jnp.bfloat16).reshape(head_shape)
    scores = attn_scores(q_heads, k_heads, score_scale)
    log_total = jax.nn.logsumexp(scores, axis=-1, keepdims=True)
    attn_probs = jnp.exp(scores - log_total).astype(jnp.bfloat16)
    attended = jnp.einsum(
        "bhqk,bkhd->bqhd", attn_probs, v_heads, preferred_element_type=jnp.float32
    )
    attended = attended.astype(jnp.bfloat16).reshape(row_count, head_cols)
    attn_total = tensor_sum(
        lambda s, w: mat_prod(attended, cols(w_out, s, w, 1)), model_width, n_tensor
    )
    resid_mid = x_rows + attn_total + out_bias
    normed2 = layer_norm(resid_mid, ln2_gain, ln2_shift).astype(jnp.bfloat16)
    pre_act = mat_prod(normed2, w_fc1) + fc1_bias
    gelu_out = quick_gelu(pre_act).astype(jnp.bfloat16)
    mlp_total = tensor_sum(
        lambda s, w: mat_prod(gelu_out, cols(w_fc2, s, w, 1)), model_width, n_tensor
    )
    block_out = (resid_mid + mlp_total + fc2_bias).astype(jnp.bfloat16).reshape(hidden_in.shape)
    out_cot = (out_grad.astype(jnp.float32) * flags.astype(jnp.float32)[:, None, None]).reshape(
        row_count, model_width
    )
    g_fc2_bias = jnp.sum(out_cot, axis=0)
    mlp_cot = out_cot.astype(jnp.bfloat16)
    g_w_fc2 = left_contract(gelu_out, mlp_cot)
    pre_grad = (right_contract(mlp_cot, w_fc2) * gelu_slope(pre_act)).astype(jnp.bfloat16)
    g_w_fc1 = left_contract(normed2, pre_grad)
    g_fc1_bias = col_sum(pre_grad)
    norm2_grad = tensor_sum(
        lambda s, w: right_contract(pre_grad, cols(w_fc1, s, w, 0)), model_width, n_tensor
    )
    unused_two, norm2_pull = jax.vjp(layer_norm, resid_mid, ln2_gain, ln2_shift)
    mid_from_norm, g_ln2_gain, g_ln2_shift = norm2_pull(norm2_grad)
    resid_grad = out_cot + mid_from_norm
    g_out_bias = jnp.sum(resid_grad, axis=0)
    attn_cot = resid_grad.astype(jnp.bfloat16)
    g_w_out = left_contract(attended, attn_cot)
    attended_grad = right_contract(attn_cot, w_out).astype(jnp.bfloat16).reshape(head_shape)
    again = attn_scores(q_heads, k_heads, score_scale)
    probs_again = jnp.exp(again - log_total)
    probs_low = probs_again.astype(jnp.bfloat16)
    probs_grad = jnp.einsum(
        "bqhd,bkhd->bhqk", attended_grad, v_heads, preferred_element_type=jnp.float32
    )
    row_dot = jnp.sum(probs_again * probs_grad, axis=-1, keepdims=True)
    score_grad = (probs_again * (probs_grad - row_dot)).astype(jnp.bfloat16)
    q_grad = (
        jnp.einsum("bhqk,bkhd->bqhd", score_grad, k_heads, preferred_element_type=jnp.float32)
        * score_scale
    ).astype(jnp.bfloat16)
    k_grad = (
        jnp.einsum("bhqk,bqhd->bkhd", score_grad, q_heads, preferred_element_type=jnp.float32)
        * score_scale
    ).astype(jnp.bfloat16)
    v_grad = jnp.einsum(
        "bhqk,bqhd->bkhd", probs_low, attended_grad, preferred_element_type=jnp.float32
    ).astype(jnp.bfloat16)
    q_rows = q_grad.reshape(row_count, head_cols)
    v_rows = v_grad.reshape(row_count, head_cols)
    qkv_grad = jnp.stack([q_rows, k_grad.reshape(row_count, head_cols), v_rows], axis=1).reshape(
        row_count, 3 * head_cols
    )
    g_w_qkv = left_contract(normed1, qkv_grad).reshape(model_width, 3, head_cols)
    g_qkv_bias = jnp.stack([col_sum(q_rows), col_sum(v_rows)], axis=0)
    norm1_grad = tensor_sum(
        lambda s, w: right_contract(qkv_grad, cols(qkv_flat, s, w, 0)), model_width, n_tensor
    )
    unused_one, norm1_pull = jax.vjp(layer_norm, x_rows, ln1_gain, ln1_shift)
    x_from_norm, g_ln1_gain, g_ln1_shift = norm1_pull(norm1_grad)
    in_grad = (resid_grad + x_from_norm).astype(jnp.bfloat16).reshape(hidden_in.shape)
    small = jnp.concatenate(
        [
            g_ln1_gain,
            g_ln1_shift,
            g_qkv_bias.reshape(-1),
            g_out_bias,
            g_ln2_gain,
            g_ln2_shift,
            g_fc1_bias,
            g_fc2_bias,
        ]
    )
    small = lax.psum(small, ("outer", "inner"))
    cuts = [model_width] * 2 + [g_qkv_bias.size] + [model_width] * 3
    cuts += [g_fc1_bias.size, model_width]
    pieces = []
    offset = 0
    for size in cuts:
        pieces.append(small[offset : offset + size])
        offset += size
    big = (g_w_qkv, g_w_out, g_w_fc1, g_w_fc2)
    big_dims = (0, 1, 0, 1)
    shares = tuple(
        lax.psum_scatter(g, "inner", scatter_dimension=d, tiled=True)
        for g, d in zip(big, big_dims)
    )
    shares = lax.psum(shares, "outer")
    summed = tuple(
        lax.all_gather(s, "inner", axis=d, tiled=True) for s, d in zip(shares, big_dims)
    )
    return (
        block_out,
        in_grad,
        pieces[0],
        pieces[1],
        summed[0],
        pieces[2].reshape(g_qkv_bias.shape),
        summed[1],
        pieces[3],
        pieces[4],
        pieces[5],
        summed[2],
        pieces[6],
        summed[3],
        pieces[7],
    )


def solution(mesh):
    placed = (
        P(("outer", "inner"), None, None),
        P(),
        P(),
        P(None, None, "tensor"),
        P(None, "tensor"),
        P("tensor", None),
        P(),
        P(),
        P(),
        P(None, "tensor"),
        P("tensor"),
        P("tensor", None),
        P(),
        P(("outer", "inner")),
        P(("outer", "inner"), None, None),
    )
    return jax.shard_map(
        functools.partial(per_device, mesh.shape["tensor"]),
        mesh=mesh,
        in_specs=placed,
        out_specs=(
            P(("outer", "inner"), None, None),
            P(("outer", "inner"), None, None),
            P(),
            P(),
            P(None, None, "tensor"),
            P(None, "tensor"),
            P("tensor", None),
            P(),
            P(),
            P(),
            P(None, "tensor"),
            P("tensor"),
            P("tensor", None),
            P(),
        ),
        check_vma=False,
    )
```
